512 devices in a mesh: spec: 4 (over y_hi, core), space: 128 (over x, z, y_lo).
Axes of the slice: x: 4, y: 4 (y_hi: 2, y_lo: 2; y = y_hi * 2 + y_lo), z: 16, core: 2. Of those that a mesh axis runs over, the one named last changes fastest.
Arguments:
- slm_phase: float32 [2048, 2048], P('space', 'spec'), as said below
- expander: int32 [8192, 512], P('space'), may hold values from 0 to 65535
- phase_scale: float32 [4], replicated, as said below
- target: float32 [64, 128, 64, 128], P(None, 'space'), may hold values from 0 to 8
Outputs:
- phase_grad: float32 [2048, 2048], P('space', 'spec')
The draws below stay inside these ranges and needn't reach their ends.
Inputs may be any that keep to these rules, and one draw needn't show every extreme that they name: Each word holds the expander bits of 16 neighbouring columns in its 16 low bits, bit j for column 16 * word + j. `slm_phase`: unwrapped phase delays between -4 pi and 4 pi radians. `phase_scale`: distinct values between 0.7 and 1.4.
All inputs are finite; a program needn't handle non-finite values.
Results may differ from the reference program's by a relative error of at most 0.025.
Values may be sent and summed in bfloat16 or wider, within the bound.
No kernel may reach another device: no remote copies, remote signals or barrier semaphores. Data moves between devices by JAX's collectives and lax.ppermute only.
A program may use at most 64 MiB of HBM per device.

```python
import math
import jax
import jax.numpy as jnp
from jax import lax

N = 8192
SUB = 64
Q1 = 128
S = 2048
WAVES = 4


def draw_slm_phase(key, part):
    return jax.random.uniform(key, (S, S), jnp.float32, -4.0 * math.pi, 4.0 * math.pi)


def draw_phase_scale(key, part):
    jitter = jax.random.uniform(jax.random.fold_in(key, 11), (WAVES,), jnp.float32, 0.0, 1.0)
    order = jax.random.permutation(jax.random.fold_in(key, 23), WAVES)
    position = (order.astype(jnp.float32) + 0.15 * jitter) / (WAVES - 1 + 0.15)
    return 0.7 * jnp.exp(position * math.log(2.0))


def with_ends(values, stream_key, smallest, largest):
    index_at = [jax.random.randint(jax.random.fold_in(stream_key, axis), (), 0, length) for axis, length in enumerate(values.shape)]
    longest = values.shape.index(max(values.shape))
    next_to = index_at[:longest] + [(index_at[longest] + 1) % values.shape[longest]] + index_at[longest + 1:]
    return values.at[tuple(index_at)].set(smallest).at[tuple(next_to)].set(largest)


def steps_of(key, shape, cuts, low, high):
    level = 1.0
    for dim, blocks in cuts:
        draws = jax.random.uniform(jax.random.fold_in(jax.random.fold_in(key, 6), dim), (blocks,), jnp.float32, low / len(cuts), high / len(cuts))
        level = level * jnp.repeat(jnp.exp(draws), shape[dim] // blocks).reshape((-1,) + (1,) * (len(shape) - 1 - dim))
    return level


def setup_inputs(seed: int = 0) -> dict:
    seeds = jax.random.split(jax.random.key(seed), 5)
    slm_phase = draw_slm_phase(jax.random.fold_in(seeds[4], 71), 0)
    expander = with_ends(jax.random.randint(seeds[1], (N, N // 16), 0, 65536), jax.random.fold_in(seeds[1], 1), 0, 65535).astype(jnp.int32)
    phase_scale = draw_phase_scale(jax.random.fold_in(seeds[4], 71), 0)
    target = jnp.clip(8.0 * jax.random.uniform(seeds[3], (SUB, Q1, SUB, Q1), jnp.float32) ** steps_of(seeds[3], (SUB, Q1, SUB, Q1), ((1, 128),), -0.2, 0.2), 0.0, 8.0)
    return dict(slm_phase=slm_phase, expander=expander, phase_scale=phase_scale, target=target)


def angle_tables(first, second, length, scale):
    row_index = jnp.arange(first, dtype=jnp.int32)[:, None]
    col_index = jnp.arange(second, dtype=jnp.int32)[None, :]
    residue = ((row_index * col_index) % length).astype(jnp.float32)
    radians = residue * (2.0 * math.pi / length)
    return jnp.cos(radians) * scale, -jnp.sin(radians) * scale


def settle(values):
    return lax.optimization_barrier(values.astype(jnp.bfloat16)).astype(jnp.float32)


def rounded_table(length):
    cos_part, sin_part = angle_tables(length, length, length, 1.0)
    return settle(cos_part), settle(sin_part)


def complex_product(pattern, left_real, left_imag, cos_table, sin_table):
    exact = lax.Precision.HIGHEST
    real_part = (jnp.einsum(pattern, left_real, cos_table, precision=exact)
                 - jnp.einsum(pattern, left_imag, sin_table, precision=exact))
    imag_part = (jnp.einsum(pattern, left_real, sin_table, precision=exact)
                 + jnp.einsum(pattern, left_imag, cos_table, precision=exact))
    return real_part, imag_part


def rotate_pair(real_in, imag_in, cos_table, sin_table):
    return real_in * cos_table - imag_in * sin_table, real_in * sin_table + imag_in * cos_table


def reference(slm_phase, expander, phase_scale, target):
    outer_len = N // SUB
    upsampled = jnp.broadcast_to(slm_phase[:, None, :, None], (S, 4, S, 4)).reshape(N, N)
    shifts = jnp.arange(16, dtype=jnp.int32)
    bit_values = jnp.bitwise_and(jnp.right_shift(expander[:, :, None], shifts), 1)
    expander_sign = (1 - 2 * bit_values).reshape(N, N).astype(jnp.float32)
    outer_cos, outer_sin = rounded_table(outer_len)
    inner_cos, inner_sin = rounded_table(SUB)
    row_cos, row_sin = angle_tables(SUB, outer_len, N, 1.0)
    col_cos, col_sin = angle_tables(SUB, outer_len, N, 1.0 / N)
    col_cos_b = col_cos[:, None, None, :]
    col_sin_b = col_sin[:, None, None, :]

    def near_of(colour):
        phase_delay = phase_scale[colour] * upsampled
        return settle(expander_sign * jnp.cos(phase_delay)), settle(expander_sign * jnp.sin(phase_delay))

    far_kept = []
    intensity = jnp.zeros((SUB, outer_len, SUB, outer_len), jnp.float32)
    for colour in range(WAVES):
        near_real, near_imag = near_of(colour)
        part_real, part_imag = complex_product("mbj,ba->mja", near_real.reshape(N, outer_len, SUB),
                                               near_imag.reshape(N, outer_len, SUB), outer_cos, outer_sin)
        part_real, part_imag = rotate_pair(part_real, part_imag, row_cos, row_sin)
        part_real, part_imag = complex_product("mja,jc->mac", settle(part_real), settle(part_imag), inner_cos, inner_sin)
        part_real = settle(part_real).reshape(outer_len, SUB, outer_len, SUB)
        part_imag = settle(part_imag).reshape(outer_len, SUB, outer_len, SUB)
        part_real, part_imag = complex_product("bjxc,bz->jxcz", part_real, part_imag, outer_cos, outer_sin)
        part_real, part_imag = rotate_pair(part_real, part_imag, col_cos_b, col_sin_b)
        far_real, far_imag = complex_product("jxcz,jy->yxcz", settle(part_real), settle(part_imag), inner_cos, inner_sin)
        far_real = settle(far_real)
        far_imag = settle(far_imag)
        far_kept.append((far_real, far_imag))
        intensity = intensity + (far_real * far_real + far_imag * far_imag)
    residual = (intensity - target) / 32.0

    slope = jnp.zeros((N, N), jnp.float32)
    for colour in range(WAVES):
        near_real, near_imag = near_of(colour)
        far_real, far_imag = far_kept[colour]
        cot_real = settle(2.0 * residual * far_real)
        cot_imag = settle(2.0 * residual * far_imag)
        part_real, part_imag = complex_product("yxcz,jy->jxcz", cot_real, cot_imag, inner_cos, -inner_sin)
        part_real, part_imag = rotate_pair(part_real, part_imag, col_cos_b, -col_sin_b)
        part_real, part_imag = complex_product("jxcz,bz->bjxc", settle(part_real), settle(part_imag), outer_cos, -outer_sin)
        part_real = settle(part_real).reshape(N, outer_len, SUB)
        part_imag = settle(part_imag).reshape(N, outer_len, SUB)
        part_real, part_imag = complex_product("mac,jc->mja", part_real, part_imag, inner_cos, -inner_sin)
        part_real, part_imag = rotate_pair(part_real, part_imag, row_cos, -row_sin)
        grad_real, grad_imag = complex_product("mja,ba->mbj", settle(part_real), settle(part_imag), outer_cos, -outer_sin)
        slope = slope + phase_scale[colour] * (grad_imag.reshape(N, N) * near_real - grad_real.reshape(N, N) * near_imag)
    return slope.reshape(S, 4, S, 4).sum(axis=(1, 3))
```

```python
import math

import jax
import jax.numpy as jnp
from jax import lax
from jax.sharding import PartitionSpec as P

N = 8192
SUB = 64
Q1 = N // SUB


def angle_tables(first, second, length, scale):
    row_index = lax.broadcasted_iota(jnp.int32, (first, second), 0)
    col_index = lax.broadcasted_iota(jnp.int32, (first, second), 1)
    residue = (row_index * col_index % length).astype(jnp.float32)
    radians = residue * (2.0 * math.pi / length)
    return (jnp.cos(radians) * scale, -jnp.sin(radians) * scale)


def transform_block(length, conjugate):
    cos_part, sin_part = angle_tables(length, length, length, 1.0)
    cos_low = cos_part.astype(jnp.bfloat16)
    sin_low = sin_part.astype(jnp.bfloat16)
    if conjugate:
        sin_low = -sin_low
    upper = jnp.concatenate([cos_low, sin_low], axis=1)
    lower = jnp.concatenate([-sin_low, cos_low], axis=1)
    return jnp.concatenate([upper, lower], axis=0)


def rotate_pair(real_in, imag_in, cos_table, sin_table):
    return (real_in * cos_table - imag_in * sin_table, real_in * sin_table + imag_in * cos_table)


def make_local(n_space, n_spec):
    both = ("space", "spec")
    n_all = n_space * n_spec

    def local(slm_phase, expander, phase_scale, target):
        waves = phase_scale.shape[0]
        rows_dev = expander.shape[0]
        rows_f = rows_dev // n_spec
        slm_rows = rows_f // 4
        lc = target.shape[1]
        cs = SUB // n_spec
        spec_index = lax.axis_index("spec")

        own_slm = lax.all_to_all(slm_phase, "spec", split_axis=0, concat_axis=1, tiled=True)
        own_exp = lax.dynamic_slice_in_dim(expander, spec_index * rows_f, rows_f, 0)

        slm_tile = own_slm.reshape(slm_rows, Q1, SUB // 4).transpose(0, 2, 1)
        upsampled = jnp.broadcast_to(
            slm_tile[:, None, :, None, :], (slm_rows, 4, SUB // 4, 4, Q1)
        ).reshape(rows_f, SUB, Q1)
        packed_words = own_exp.reshape(rows_f, Q1, SUB // 16).transpose(0, 2, 1)
        shifts = lax.broadcasted_iota(jnp.int32, (1, 1, 16, 1), 2)
        bit_values = jnp.bitwise_and(jnp.right_shift(packed_words[:, :, None, :], shifts), 1)
        expander_sign = (1 - 2 * bit_values).reshape(rows_f, SUB, Q1).astype(jnp.float32)
        phase_delay = phase_scale[:, None, None, None] * upsampled[None]
        near_real = (expander_sign[None] * jnp.cos(phase_delay)).astype(jnp.bfloat16)
        near_imag = (expander_sign[None] * jnp.sin(phase_delay)).astype(jnp.bfloat16)
        near_field = jnp.concatenate([near_real, near_imag], axis=-1)

        outer_fwd = transform_block(Q1, False)
        outer_inv = transform_block(Q1, True)
        inner_fwd = transform_block(SUB, False)
        inner_inv = transform_block(SUB, True)
        row_cos, row_sin = angle_tables(SUB, Q1, N, 1.0)
        col_cos, col_sin = angle_tables(SUB, Q1, N, 1.0 / N)
        col_cos_b = col_cos[:, None, None, None, :]
        col_sin_b = col_sin[:, None, None, None, :]

        batch = waves * rows_f
        section_out = jnp.dot(
            near_field.reshape(batch * SUB, 2 * Q1), outer_fwd, preferred_element_type=jnp.float32
        ).reshape(batch, SUB, 2, Q1)
        first_real, first_imag = rotate_pair(
            section_out[:, :, 0], section_out[:, :, 1], row_cos, row_sin
        )
        first_part = jnp.stack(
            [first_real.transpose(0, 2, 1), first_imag.transpose(0, 2, 1)], axis=2
        ).astype(jnp.bfloat16)
        row_freq = (
            jnp.dot(
                first_part.reshape(batch * Q1, 2 * SUB), inner_fwd, preferred_element_type=jnp.float32
            )
            .astype(jnp.bfloat16)
            .reshape(waves, rows_f, n_space, lc, 2, n_spec, cs)
        )
        send = row_freq.transpose(2, 5, 0, 1, 3, 4, 6).reshape(n_all, -1)
        got = lax.all_to_all(send, both, split_axis=0, concat_axis=0, tiled=True)
        columns = got.reshape(n_all, waves, rows_f, lc, 2, cs).transpose(1, 0, 2, 3, 4, 5)
        columns = columns.reshape(waves, Q1, SUB, lc, 2, cs).transpose(2, 0, 3, 5, 4, 1)
        columns = columns.reshape(SUB * waves * lc * cs, 2 * Q1)
        section_out = jnp.dot(columns, outer_fwd, preferred_element_type=jnp.float32).reshape(
            SUB, waves, lc, cs, 2, Q1
        )
        col_real, col_imag = rotate_pair(
            section_out[:, :, :, :, 0], section_out[:, :, :, :, 1], col_cos_b, col_sin_b
        )
        col_first = (
            jnp.stack([col_real, col_imag], axis=0)
            .astype(jnp.bfloat16)
            .reshape(2 * SUB, waves * lc * cs * Q1)
        )
        far_field = jnp.dot(inner_inv, col_first, preferred_element_type=jnp.float32).astype(
            jnp.bfloat16
        )
        far_wide = far_field.astype(jnp.float32).reshape(2, SUB, waves, lc, cs, Q1)
        power = jnp.sum(far_wide[0] * far_wide[0] + far_wide[1] * far_wide[1], axis=1)
        own_target = lax.dynamic_slice_in_dim(target, spec_index * cs, cs, 2)
        residual = (power - own_target) / 32.0
        cotangent = (2.0 * residual[None, :, None] * far_wide).astype(jnp.bfloat16)
        back_out = jnp.dot(
            inner_fwd,
            cotangent.reshape(2 * SUB, waves * lc * cs * Q1),
            preferred_element_type=jnp.float32,
        ).reshape(2, SUB, waves, lc, cs, Q1)
        back_real, back_imag = rotate_pair(back_out[0], back_out[1], col_cos_b, -col_sin_b)
        back_one = (
            jnp.stack([back_real, back_imag], axis=4)
            .astype(jnp.bfloat16)
            .reshape(SUB * waves * lc * cs, 2 * Q1)
        )
        back_two = jnp.dot(back_one, outer_inv, preferred_element_type=jnp.float32).astype(jnp.bfloat16)
        back_two = back_two.reshape(SUB, waves, lc, cs, 2, Q1).transpose(1, 5, 0, 2, 4, 3)
        back_two = back_two.reshape(waves, n_all, rows_f, lc, 2, cs).transpose(1, 0, 2, 3, 4, 5)
        rows_back = lax.all_to_all(
            back_two.reshape(n_all, -1), both, split_axis=0, concat_axis=0, tiled=True
        )
        rows_back = rows_back.reshape(n_space, n_spec, waves, rows_f, lc, 2, cs)
        rows_back = rows_back.transpose(2, 3, 0, 4, 5, 1, 6).reshape(batch * Q1, 2 * SUB)
        section_out = jnp.dot(rows_back, inner_inv, preferred_element_type=jnp.float32).reshape(
            batch, Q1, 2, SUB
        )
        turned_real, turned_imag = rotate_pair(
            section_out[:, :, 0], section_out[:, :, 1], row_cos.T, -row_sin.T
        )
        back_three = jnp.stack(
            [turned_real.transpose(0, 2, 1), turned_imag.transpose(0, 2, 1)], axis=2
        ).astype(jnp.bfloat16)
        near_grad = jnp.dot(
            back_three.reshape(batch * SUB, 2 * Q1), outer_inv, preferred_element_type=jnp.float32
        ).reshape(waves, rows_f, SUB, 2, Q1)
        near_wide = near_field.astype(jnp.float32).reshape(waves, rows_f, SUB, 2, Q1)
        slope = jnp.sum(
            phase_scale[:, None, None, None]
            * (near_grad[:, :, :, 1] * near_wide[:, :, :, 0] - near_grad[:, :, :, 0] * near_wide[:, :, :, 1]),
            axis=0,
        )
        pooled = slope.reshape(slm_rows, 4, SUB // 4, 4, Q1).sum(axis=(1, 3)).transpose(0, 2, 1)
        pooled = pooled.reshape(slm_rows, N // 4)
        return lax.all_to_all(pooled, "spec", split_axis=1, concat_axis=0, tiled=True)

    return local


def solution(mesh):
    return jax.shard_map(
        make_local(mesh.shape["space"], mesh.shape["spec"]),
        mesh=mesh,
        in_specs=(P("space", "spec"), P("space", None), P(), P(None, "space", None, None)),
        out_specs=P("space", "spec"),
        check_vma=False,
    )
```

```python
import math

import jax
import jax.numpy as jnp
from jax import lax
from jax.sharding import PartitionSpec as P

N = 8192
SUB = 64
Q1 = N // SUB


def angle_tables(first, second, length, scale):
    row_index = lax.broadcasted_iota(jnp.int32, (first, second), 0)
    col_index = lax.broadcasted_iota(jnp.int32, (first, second), 1)
    residue = (row_index * col_index % length).astype(jnp.float32)
    radians = residue * (2.0 * math.pi / length)
    return (jnp.cos(radians) * scale, -jnp.sin(radians) * scale)


def transform_block(length, conjugate):
    cos_part, sin_part = angle_tables(length, length, length, 1.0)
    cos_low = cos_part.astype(jnp.bfloat16)
    sin_low = sin_part.astype(jnp.bfloat16)
    if conjugate:
        sin_low = -sin_low
    upper = jnp.concatenate([cos_low, sin_low], axis=1)
    lower = jnp.concatenate([-sin_low, cos_low], axis=1)
    return jnp.concatenate([upper, lower], axis=0)


def rotate_pair(real_in, imag_in, cos_table, sin_table):
    return (real_in * cos_table - imag_in * sin_table, real_in * sin_table + imag_in * cos_table)


def make_local(n_space, n_spec):
    both = ("space", "spec")
    n_all = n_space * n_spec

    def local(slm_phase, expander, phase_scale, target):
        waves = phase_scale.shape[0]
        rows_dev = expander.shape[0]
        rows_f = rows_dev // n_spec
        slm_rows = rows_f // 4
        lc = target.shape[1]
        cs = SUB // n_spec
        kk = lc * cs
        group = SUB // rows_f
        batch = waves * rows_f
        spec_index = lax.axis_index("spec")

        own_slm = lax.all_to_all(slm_phase, "spec", split_axis=0, concat_axis=1, tiled=True)
        own_exp = lax.dynamic_slice_in_dim(expander, spec_index * rows_f, rows_f, 0)

        slm_tile = own_slm.reshape(slm_rows, Q1, SUB // 4).transpose(0, 2, 1)
        upsampled = jnp.broadcast_to(
            slm_tile[:, None, :, None, :], (slm_rows, 4, SUB // 4, 4, Q1)
        ).reshape(rows_f, SUB, Q1)
        packed_words = own_exp.reshape(rows_f, Q1, SUB // 16).transpose(0, 2, 1)
        shifts = lax.broadcasted_iota(jnp.int32, (1, 1, 16, 1), 2)
        bit_values = jnp.bitwise_and(jnp.right_shift(packed_words[:, :, None, :], shifts), 1)
        expander_sign = (1 - 2 * bit_values).reshape(rows_f, SUB, Q1).astype(jnp.float32)
        phase_delay = phase_scale[:, None, None, None] * upsampled[None]
        near_real = (expander_sign[None] * jnp.cos(phase_delay)).astype(jnp.bfloat16)
        near_imag = (expander_sign[None] * jnp.sin(phase_delay)).astype(jnp.bfloat16)
        near_field = jnp.concatenate([near_real, near_imag], axis=-1).reshape(batch * SUB, 2 * Q1)

        outer_fwd = transform_block(Q1, False)
        outer_inv = transform_block(Q1, True)
        inner_fwd = transform_block(SUB, False)
        inner_inv = transform_block(SUB, True)
        row_cos, row_sin = angle_tables(SUB, Q1, N, 1.0)

        section_out = jnp.dot(near_field, outer_fwd, preferred_element_type=jnp.float32)
        section_out = section_out.reshape(batch, SUB, 2, Q1)
        first_real, first_imag = rotate_pair(
            section_out[:, :, 0], section_out[:, :, 1], row_cos, row_sin
        )
        first_part = jnp.stack([first_real, first_imag], axis=1).astype(jnp.bfloat16)
        first_part = first_part.reshape(batch, 2 * SUB, Q1)
        row_freq = jnp.einsum(
            "xk,bxa->kba", inner_fwd, first_part, preferred_element_type=jnp.float32
        ).astype(jnp.bfloat16)
        send = row_freq.reshape(2, n_spec, cs, batch, n_space, lc)
        send = send.transpose(4, 1, 0, 5, 2, 3).reshape(n_all, 16, -1)
        got = lax.all_to_all(send, both, split_axis=0, concat_axis=0, tiled=True)
        columns = got.reshape(Q1, group, 2, kk * batch).transpose(2, 0, 1, 3)
        columns = columns.reshape(2 * Q1, group * kk * batch)
        col_sec = jnp.einsum("xk,xy->ky", outer_fwd, columns, preferred_element_type=jnp.float32)
        col_sec = col_sec.reshape(2, Q1, group, kk * waves, rows_f)
        a2_index = lax.broadcasted_iota(jnp.int32, (Q1, group, 1, rows_f), 0)
        j2_index = (lax.broadcasted_iota(jnp.int32, (Q1, group, 1, rows_f), 1) * rows_f
                    + lax.broadcasted_iota(jnp.int32, (Q1, group, 1, rows_f), 3))
        col_angle = ((a2_index * j2_index) % N).astype(jnp.float32) * (2.0 * math.pi / N)
        g_cos = jnp.cos(col_angle) / N
        g_sin = -jnp.sin(col_angle) / N
        col_real, col_imag = rotate_pair(col_sec[0], col_sec[1], g_cos, g_sin)
        col_first = jnp.stack([col_real, col_imag], axis=0).astype(jnp.bfloat16)
        col_first = col_first.transpose(0, 2, 4, 3, 1).reshape(2 * SUB, kk * waves * Q1)
        far_field = jnp.dot(inner_inv, col_first, preferred_element_type=jnp.float32).astype(
            jnp.bfloat16
        )
        far_wide = far_field.astype(jnp.float32).reshape(2, SUB, kk, waves, Q1)
        power = jnp.sum(far_wide[0] * far_wide[0] + far_wide[1] * far_wide[1], axis=2)
        own_target = target.reshape(SUB, lc, n_spec, cs, Q1)
        own_target = lax.dynamic_index_in_dim(own_target, spec_index, 2, keepdims=False)
        residual = (power - own_target.reshape(SUB, kk, Q1)) / 32.0
        cotangent = (2.0 * residual[None, :, :, None] * far_wide).astype(jnp.bfloat16)
        back_out = jnp.dot(
            inner_fwd, cotangent.reshape(2 * SUB, kk * waves * Q1), preferred_element_type=jnp.float32
        ).reshape(2, SUB, kk * waves, Q1)
        gb_cos = g_cos.reshape(Q1, SUB).T[:, None, :]
        gb_sin = g_sin.reshape(Q1, SUB).T[:, None, :]
        back_real, back_imag = rotate_pair(back_out[0], back_out[1], gb_cos, -gb_sin)
        back_one = jnp.stack([back_real, back_imag], axis=0).astype(jnp.bfloat16)
        back_one = back_one.reshape(2, group, rows_f, kk, waves, Q1).transpose(0, 5, 1, 3, 2, 4)
        back_one = back_one.reshape(2 * Q1, group * kk * batch)
        back_two = jnp.einsum(
            "xk,xy->ky", outer_inv, back_one, preferred_element_type=jnp.float32
        ).astype(jnp.bfloat16)
        back_two = back_two.reshape(2, Q1, group, kk * batch).transpose(1, 2, 0, 3)
        rows_back = lax.all_to_all(
            back_two.reshape(n_all, 16, -1), both, split_axis=0, concat_axis=0, tiled=True
        )
        rows_back = rows_back.reshape(n_space, n_spec, 2, lc, cs, rows_f * waves)
        rows_back = rows_back.transpose(2, 1, 4, 5, 0, 3).reshape(2 * SUB, batch * Q1)
        section_out = jnp.einsum(
            "xk,xy->ky", inner_inv, rows_back, preferred_element_type=jnp.float32
        ).reshape(2, SUB, batch, Q1)
        rb_cos = row_cos[:, None, :]
        rb_sin = row_sin[:, None, :]
        turned_real, turned_imag = rotate_pair(section_out[0], section_out[1], rb_cos, -rb_sin)
        back_three = jnp.stack([turned_real, turned_imag], axis=0).astype(jnp.bfloat16)
        back_three = back_three.reshape(2, SUB, rows_f, waves, Q1).transpose(3, 2, 1, 0, 4)
        back_three = back_three.reshape(batch * SUB, 2 * Q1)
        near_grad = jnp.dot(back_three, outer_inv, preferred_element_type=jnp.float32).reshape(
            waves, rows_f, SUB, 2, Q1
        )
        near_wide = near_field.astype(jnp.float32).reshape(waves, rows_f, SUB, 2, Q1)
        slope = jnp.sum(
            phase_scale[:, None, None, None]
            * (near_grad[:, :, :, 1] * near_wide[:, :, :, 0] - near_grad[:, :, :, 0] * near_wide[:, :, :, 1]),
            axis=0,
        )
        pooled = slope.reshape(slm_rows, 4, SUB // 4, 4, Q1).sum(axis=(1, 3)).transpose(0, 2, 1)
        pooled = pooled.reshape(slm_rows, N // 4)
        return lax.all_to_all(pooled, "spec", split_axis=1, concat_axis=0, tiled=True)

    return local


def solution(mesh):
    return jax.shard_map(
        make_local(mesh.shape["space"], mesh.shape["spec"]),
        mesh=mesh,
        in_specs=(P("space", "spec"), P("space", None), P(), P(None, "space", None, None)),
        out_specs=P("space", "spec"),
        check_vma=False,
    )
```

```python
import math

import jax
import jax.numpy as jnp
from jax import lax
from jax.sharding import PartitionSpec as P

N = 8192
SUB = 64
Q1 = N // SUB


def angle_tables(first, second, length, scale):
    row_index = lax.broadcasted_iota(jnp.int32, (first, second), 0)
    col_index = lax.broadcasted_iota(jnp.int32, (first, second), 1)
    residue = (row_index * col_index % length).astype(jnp.float32)
    radians = residue * (2.0 * math.pi / length)
    return (jnp.cos(radians) * scale, -jnp.sin(radians) * scale)


def transform_block(length, conjugate):
    cos_part, sin_part = angle_tables(length, length, length, 1.0)
    cos_low = cos_part.astype(jnp.bfloat16)
    sin_low = sin_part.astype(jnp.bfloat16)
    if conjugate:
        sin_low = -sin_low
    upper = jnp.concatenate([cos_low, sin_low], axis=1)
    lower = jnp.concatenate([-sin_low, cos_low], axis=1)
    return jnp.concatenate([upper, lower], axis=0)


def rotate_pair(real_in, imag_in, cos_table, sin_table):
    return (real_in * cos_table - imag_in * sin_table, real_in * sin_table + imag_in * cos_table)


def make_local(n_space, n_spec):
    both = ("space", "spec")
    n_all = n_space * n_spec

    def local(slm_phase, expander, phase_scale, target):
        waves = phase_scale.shape[0]
        rows_dev = expander.shape[0]
        rows_f = rows_dev // n_spec
        slm_rows = rows_f // 4
        lc = target.shape[1]
        cs = SUB // n_spec
        kk = lc * cs
        group = SUB // rows_f
        batch = waves * rows_f
        spec_index = lax.axis_index("spec")

        own_slm = lax.all_to_all(slm_phase, "spec", split_axis=0, concat_axis=1, tiled=True)
        own_exp = lax.dynamic_slice_in_dim(expander, spec_index * rows_f, rows_f, 0)

        slm_tile = own_slm.reshape(slm_rows, Q1, SUB // 4).transpose(0, 2, 1)
        upsampled = jnp.broadcast_to(
            slm_tile[:, None, :, None, :], (slm_rows, 4, SUB // 4, 4, Q1)
        ).reshape(rows_f, SUB, Q1)
        packed_words = own_exp.reshape(rows_f, Q1, SUB // 16).transpose(0, 2, 1)
        shifts = lax.broadcasted_iota(jnp.int32, (1, 1, 16, 1), 2)
        bit_values = jnp.bitwise_and(jnp.right_shift(packed_words[:, :, None, :], shifts), 1)
        expander_sign = (1 - 2 * bit_values).reshape(rows_f, SUB, Q1).astype(jnp.float32)
        phase_delay = phase_scale[:, None, None, None] * upsampled[None]
        near_real = (expander_sign[None] * jnp.cos(phase_delay)).astype(jnp.bfloat16)
        near_imag = (expander_sign[None] * jnp.sin(phase_delay)).astype(jnp.bfloat16)
        near_field = jnp.concatenate([near_real, near_imag], axis=-1).reshape(batch * SUB, 2 * Q1)

        outer_fwd = transform_block(Q1, False)
        outer_inv = transform_block(Q1, True)
        inner_fwd = transform_block(SUB, False)
        inner_inv = transform_block(SUB, True)
        row_cos, row_sin = angle_tables(SUB, Q1, N, 1.0)

        section_out = jnp.dot(near_field, outer_fwd, preferred_element_type=jnp.float32)
        section_out = section_out.reshape(batch, SUB, 2, Q1)
        first_real, first_imag = rotate_pair(
            section_out[:, :, 0], section_out[:, :, 1], row_cos, row_sin
        )
        first_part = jnp.stack([first_real, first_imag], axis=1).astype(jnp.bfloat16)
        first_part = first_part.reshape(batch, 2 * SUB, Q1)
        row_freq = jnp.einsum(
            "xk,bxa->kba", inner_fwd, first_part, preferred_element_type=jnp.float32
        ).astype(jnp.bfloat16)
        chunks = 2 if waves % 2 == 0 else 1
        hw = waves // chunks
        hb = hw * rows_f
        payload = 2 * kk * hb
        tile_rows = payload // 128 if payload % 128 == 0 else 1
        row_freq = row_freq.reshape(2 * SUB, chunks, hb, Q1)
        a2_index = lax.broadcasted_iota(jnp.int32, (Q1, group, 1, rows_f), 0)
        j2_index = (lax.broadcasted_iota(jnp.int32, (Q1, group, 1, rows_f), 1) * rows_f
                    + lax.broadcasted_iota(jnp.int32, (Q1, group, 1, rows_f), 3))
        col_angle = ((a2_index * j2_index) % N).astype(jnp.float32) * (2.0 * math.pi / N)
        g_cos = jnp.cos(col_angle) / N
        g_sin = -jnp.sin(col_angle) / N

        far_parts = []
        power = None
        for h in range(chunks):
            send = row_freq[:, h].reshape(2, n_spec, cs, hb, n_space, lc)
            send = send.transpose(4, 1, 0, 5, 2, 3).reshape(n_all, tile_rows, -1)
            got = lax.all_to_all(send, both, split_axis=0, concat_axis=0, tiled=True)
            columns = got.reshape(Q1, group, 2, kk * hb).transpose(2, 0, 1, 3)
            columns = columns.reshape(2 * Q1, group * kk * hb)
            col_sec = jnp.einsum("xk,xy->ky", outer_fwd, columns, preferred_element_type=jnp.float32)
            col_sec = col_sec.reshape(2, Q1, group, kk * hw, rows_f)
            col_real, col_imag = rotate_pair(col_sec[0], col_sec[1], g_cos, g_sin)
            col_first = jnp.stack([col_real, col_imag], axis=0).astype(jnp.bfloat16)
            col_first = col_first.transpose(0, 2, 4, 3, 1).reshape(2 * SUB, kk * hw * Q1)
            far_field = jnp.dot(inner_inv, col_first, preferred_element_type=jnp.float32).astype(
                jnp.bfloat16
            )
            far_wide = far_field.astype(jnp.float32).reshape(2, SUB, kk, hw, Q1)
            far_parts.append(far_wide)
            part = jnp.sum(far_wide[0] * far_wide[0] + far_wide[1] * far_wide[1], axis=2)
            power = part if power is None else power + part
        own_target = target.reshape(SUB, lc, n_spec, cs, Q1)
        own_target = lax.dynamic_index_in_dim(own_target, spec_index, 2, keepdims=False)
        residual = (power - own_target.reshape(SUB, kk, Q1)) / 32.0
        gb_cos = g_cos.reshape(Q1, SUB).T[:, None, :]
        gb_sin = g_sin.reshape(Q1, SUB).T[:, None, :]
        rb_cos = row_cos[:, None, :]
        rb_sin = row_sin[:, None, :]
        near_rows = near_field.reshape(chunks, hb * SUB, 2 * Q1)
        scale_rows = phase_scale.reshape(chunks, hw)

        slope = None
        for h in range(chunks):
            cotangent = (2.0 * residual[None, :, :, None] * far_parts[h]).astype(jnp.bfloat16)
            back_out = jnp.dot(
                inner_fwd, cotangent.reshape(2 * SUB, kk * hw * Q1), preferred_element_type=jnp.float32
            ).reshape(2, SUB, kk * hw, Q1)
            back_real, back_imag = rotate_pair(back_out[0], back_out[1], gb_cos, -gb_sin)
            back_one = jnp.stack([back_real, back_imag], axis=0).astype(jnp.bfloat16)
            back_one = back_one.reshape(2, group, rows_f, kk, hw, Q1).transpose(0, 5, 1, 3, 2, 4)
            back_one = back_one.reshape(2 * Q1, group * kk * hb)
            back_two = jnp.einsum(
                "xk,xy->ky", outer_inv, back_one, preferred_element_type=jnp.float32
            ).astype(jnp.bfloat16)
            back_two = back_two.reshape(2, Q1, group, kk * hb).transpose(1, 2, 0, 3)
            rows_back = lax.all_to_all(
                back_two.reshape(n_all, tile_rows, -1), both, split_axis=0, concat_axis=0, tiled=True
            )
            rows_back = rows_back.reshape(n_space, n_spec, 2, lc, cs, rows_f * hw)
            rows_back = rows_back.transpose(2, 1, 4, 5, 0, 3).reshape(2 * SUB, hb * Q1)
            section_out = jnp.einsum(
                "xk,xy->ky", inner_inv, rows_back, preferred_element_type=jnp.float32
            ).reshape(2, SUB, hb, Q1)
            turned_real, turned_imag = rotate_pair(section_out[0], section_out[1], rb_cos, -rb_sin)
            back_three = jnp.stack([turned_real, turned_imag], axis=0).astype(jnp.bfloat16)
            back_three = back_three.reshape(2, SUB, rows_f, hw, Q1).transpose(3, 2, 1, 0, 4)
            back_three = back_three.reshape(hb * SUB, 2 * Q1)
            near_grad = jnp.dot(back_three, outer_inv, preferred_element_type=jnp.float32).reshape(
                hw, rows_f, SUB, 2, Q1
            )
            near_wide = near_rows[h].astype(jnp.float32).reshape(hw, rows_f, SUB, 2, Q1)
            part = jnp.sum(
                scale_rows[h][:, None, None, None]
                * (near_grad[:, :, :, 1] * near_wide[:, :, :, 0] - near_grad[:, :, :, 0] * near_wide[:, :, :, 1]),
                axis=0,
            )
            slope = part if slope is None else slope + part
        pooled = slope.reshape(slm_rows, 4, SUB // 4, 4, Q1).sum(axis=(1, 3)).transpose(0, 2, 1)
        pooled = pooled.reshape(slm_rows, N // 4)
        return lax.all_to_all(pooled, "spec", split_axis=1, concat_axis=0, tiled=True)

    return local


def solution(mesh):
    return jax.shard_map(
        make_local(mesh.shape["space"], mesh.shape["spec"]),
        mesh=mesh,
        in_specs=(P("space", "spec"), P("space", None), P(), P(None, "space", None, None)),
        out_specs=P("space", "spec"),
        check_vma=False,
    )
```

```python
import math

import jax
import jax.numpy as jnp
from jax import lax
from jax.sharding import PartitionSpec as P

N = 8192
SUB = 64
Q1 = N // SUB


def angle_tables(first, second, length, scale):
    row_index = lax.broadcasted_iota(jnp.int32, (first, second), 0)
    col_index = lax.broadcasted_iota(jnp.int32, (first, second), 1)
    residue = (row_index * col_index % length).astype(jnp.float32)
    radians = residue * (2.0 * math.pi / length)
    return (jnp.cos(radians) * scale, -jnp.sin(radians) * scale)


def transform_block(length, conjugate):
    cos_part, sin_part = angle_tables(length, length, length, 1.0)
    cos_low = cos_part.astype(jnp.bfloat16)
    sin_low = sin_part.astype(jnp.bfloat16)
    if conjugate:
        sin_low = -sin_low
    upper = jnp.concatenate([cos_low, sin_low], axis=1)
    lower = jnp.concatenate([-sin_low, cos_low], axis=1)
    return jnp.concatenate([upper, lower], axis=0)


def rotate_pair(real_in, imag_in, cos_table, sin_table):
    return (real_in * cos_table - imag_in * sin_table, real_in * sin_table + imag_in * cos_table)


def make_local(n_space, n_spec):
    both = ("space", "spec")
    n_all = n_space * n_spec

    def local(slm_phase, expander, phase_scale, target):
        waves = phase_scale.shape[0]
        rows_dev = expander.shape[0]
        rows_f = rows_dev // n_spec
        slm_rows = rows_f // 4
        lc = target.shape[1]
        cs = SUB // n_spec
        kk = lc * cs
        group = SUB // rows_f
        batch = waves * rows_f
        spec_index = lax.axis_index("spec")

        own_slm = lax.all_to_all(slm_phase, "spec", split_axis=0, concat_axis=1, tiled=True)
        own_exp = lax.dynamic_slice_in_dim(expander, spec_index * rows_f, rows_f, 0)

        slm_tile = own_slm.reshape(slm_rows, Q1, SUB // 4).transpose(0, 2, 1)
        upsampled = jnp.broadcast_to(
            slm_tile[:, None, :, None, :], (slm_rows, 4, SUB // 4, 4, Q1)
        ).reshape(rows_f, SUB, Q1)
        packed_words = own_exp.reshape(rows_f, Q1, SUB // 16).transpose(0, 2, 1)
        shifts = lax.broadcasted_iota(jnp.int32, (1, 1, 16, 1), 2)
        bit_values = jnp.bitwise_and(jnp.right_shift(packed_words[:, :, None, :], shifts), 1)
        expander_sign = (1 - 2 * bit_values).reshape(rows_f, SUB, Q1).astype(jnp.float32)
        phase_delay = phase_scale[:, None, None, None] * upsampled[None]
        near_real = (expander_sign[None] * jnp.cos(phase_delay)).astype(jnp.bfloat16)
        near_imag = (expander_sign[None] * jnp.sin(phase_delay)).astype(jnp.bfloat16)
        near_field = jnp.concatenate([near_real, near_imag], axis=-1).reshape(batch * SUB, 2 * Q1)
        near_field = lax.optimization_barrier(near_field)

        outer_fwd = transform_block(Q1, False)
        outer_inv = transform_block(Q1, True)
        inner_fwd = transform_block(SUB, False)
        inner_inv = transform_block(SUB, True)
        row_cos, row_sin = angle_tables(SUB, Q1, N, 1.0)

        section_out = jnp.dot(near_field, outer_fwd, preferred_element_type=jnp.float32)
        first_real, first_imag = rotate_pair(
            section_out[:, :Q1].reshape(batch, SUB, Q1),
            section_out[:, Q1:].reshape(batch, SUB, Q1),
            row_cos,
            row_sin,
        )
        first_part = jnp.stack([first_real, first_imag], axis=1).astype(jnp.bfloat16)
        first_part = first_part.reshape(batch, 2 * SUB, Q1)
        row_freq = jnp.einsum(
            "xk,bxa->kba", inner_fwd, first_part, preferred_element_type=jnp.float32
        ).astype(jnp.bfloat16)
        send = row_freq.reshape(2, n_spec, cs, batch, n_space, lc)
        send = send.transpose(4, 1, 0, 5, 2, 3).reshape(n_all, 16, -1)
        got = lax.all_to_all(send, both, split_axis=0, concat_axis=0, tiled=True)
        columns = got.reshape(Q1, group, 2, kk * batch).transpose(2, 0, 1, 3)
        columns = columns.reshape(2 * Q1, group * kk * batch)
        col_sec = jnp.einsum("xk,xy->ky", outer_fwd, columns, preferred_element_type=jnp.float32)
        col_sec = col_sec.reshape(2, Q1, group, kk, waves, rows_f)
        a2_index = lax.broadcasted_iota(jnp.int32, (Q1, group, 1, 1, rows_f), 0)
        j2_index = (lax.broadcasted_iota(jnp.int32, (Q1, group, 1, 1, rows_f), 1) * rows_f
                    + lax.broadcasted_iota(jnp.int32, (Q1, group, 1, 1, rows_f), 4))
        col_angle = ((a2_index * j2_index) % N).astype(jnp.float32) * (2.0 * math.pi / N)
        g_cos = jnp.cos(col_angle) / N
        g_sin = -jnp.sin(col_angle) / N
        col_real, col_imag = rotate_pair(col_sec[0], col_sec[1], g_cos, g_sin)
        col_first = jnp.stack([col_real, col_imag], axis=0).astype(jnp.bfloat16)
        col_first = col_first.transpose(0, 2, 5, 4, 3, 1).reshape(2 * SUB, waves * kk * Q1)
        far_field = jnp.dot(inner_inv, col_first, preferred_element_type=jnp.float32).astype(
            jnp.bfloat16
        )
        far_wide = far_field.astype(jnp.float32).reshape(2, SUB, waves, kk, Q1)
        power = jnp.sum(far_wide[0] * far_wide[0] + far_wide[1] * far_wide[1], axis=1)
        own_target = target.reshape(SUB, lc, n_spec, cs, Q1)
        own_target = lax.dynamic_index_in_dim(own_target, spec_index, 2, keepdims=False)
        residual = (power - own_target.reshape(SUB, kk, Q1)) / 32.0
        cotangent = (2.0 * residual[None, :, None] * far_wide).astype(jnp.bfloat16)
        back_out = jnp.dot(
            inner_fwd, cotangent.reshape(2 * SUB, kk * waves * Q1), preferred_element_type=jnp.float32
        ).reshape(2, SUB, kk * waves, Q1)
        gb_cos = g_cos.reshape(Q1, SUB).T[:, None, :]
        gb_sin = g_sin.reshape(Q1, SUB).T[:, None, :]
        back_real, back_imag = rotate_pair(back_out[0], back_out[1], gb_cos, -gb_sin)
        back_one = jnp.stack([back_real, back_imag], axis=0).astype(jnp.bfloat16)
        back_one = back_one.reshape(2, group, rows_f, waves, kk, Q1).transpose(0, 5, 1, 4, 2, 3)
        back_one = back_one.reshape(2 * Q1, group * kk * batch)
        back_two = jnp.einsum(
            "xk,xy->ky", outer_inv, back_one, preferred_element_type=jnp.float32
        ).astype(jnp.bfloat16)
        back_two = back_two.reshape(2, Q1, group, kk * batch).transpose(1, 2, 0, 3)
        rows_back = lax.all_to_all(
            back_two.reshape(n_all, 16, -1), both, split_axis=0, concat_axis=0, tiled=True
        )
        rows_back = rows_back.reshape(n_space, n_spec, 2, lc, cs, rows_f * waves)
        rows_back = rows_back.transpose(2, 1, 4, 5, 0, 3).reshape(2 * SUB, batch * Q1)
        section_out = jnp.einsum(
            "xk,xy->ky", inner_inv, rows_back, preferred_element_type=jnp.float32
        ).reshape(2, SUB, batch, Q1)
        rb_cos = row_cos[:, None, :]
        rb_sin = row_sin[:, None, :]
        turned_real, turned_imag = rotate_pair(section_out[0], section_out[1], rb_cos, -rb_sin)
        back_three = jnp.stack([turned_real, turned_imag], axis=0).astype(jnp.bfloat16)
        back_three = back_three.reshape(2, SUB, rows_f, waves, Q1).transpose(3, 2, 1, 0, 4)
        back_three = back_three.reshape(batch * SUB, 2 * Q1)
        near_grad = jnp.dot(back_three, outer_inv, preferred_element_type=jnp.float32).reshape(
            waves, rows_f * SUB, 2 * Q1
        )
        near_wide = near_field.reshape(waves, rows_f * SUB, 2 * Q1).astype(jnp.float32)
        slope = jnp.sum(
            phase_scale[:, None, None]
            * (near_grad[:, :, Q1:] * near_wide[:, :, :Q1] - near_grad[:, :, :Q1] * near_wide[:, :, Q1:]),
            axis=0,
        )
        pooled = slope.reshape(slm_rows, 4, SUB // 4, 4, Q1).sum(axis=(1, 3)).transpose(0, 2, 1)
        pooled = pooled.reshape(slm_rows, N // 4)
        return lax.all_to_all(pooled, "spec", split_axis=1, concat_axis=0, tiled=True)

    return local


def solution(mesh):
    return jax.shard_map(
        make_local(mesh.shape["space"], mesh.shape["spec"]),
        mesh=mesh,
        in_specs=(P("space", "spec"), P("space", None), P(), P(None, "space", None, None)),
        out_specs=P("space", "spec"),
        check_vma=False,
    )
```

```python
import math

import jax
import jax.numpy as jnp
from jax import lax
from jax.sharding import PartitionSpec as P

N = 8192
SUB = 64
Q1 = N // SUB


def angle_tables(first, second, length, scale):
    row_index = lax.broadcasted_iota(jnp.int32, (first, second), 0)
    col_index = lax.broadcasted_iota(jnp.int32, (first, second), 1)
    residue = (row_index * col_index % length).astype(jnp.float32)
    radians = residue * (2.0 * math.pi / length)
    return (jnp.cos(radians) * scale, -jnp.sin(radians) * scale)


def transform_block(length, conjugate):
    cos_part, sin_part = angle_tables(length, length, length, 1.0)
    cos_low = cos_part.astype(jnp.bfloat16)
    sin_low = sin_part.astype(jnp.bfloat16)
    if conjugate:
        sin_low = -sin_low
    upper = jnp.concatenate([cos_low, sin_low], axis=1)
    lower = jnp.concatenate([-sin_low, cos_low], axis=1)
    return jnp.concatenate([upper, lower], axis=0)


def rotate_pair(real_in, imag_in, cos_table, sin_table):
    return (real_in * cos_table - imag_in * sin_table, real_in * sin_table + imag_in * cos_table)


def spec_exchange(x, n_spec, split_axis, concat_axis):
    me = lax.axis_index("spec")
    size = x.shape[split_axis] // n_spec
    pieces = []
    for shift in range(n_spec):
        target = (me + shift) % n_spec
        piece = lax.dynamic_slice_in_dim(x, target * size, size, split_axis)
        if shift:
            pairs = [(src, (src + shift) % n_spec) for src in range(n_spec)]
            piece = lax.ppermute(piece, "spec", pairs)
        pieces.append(piece)
    stacked = jnp.stack(pieces, axis=0)
    order = (me - jnp.arange(n_spec)) % n_spec
    ordered = jnp.take(stacked, order, axis=0)
    ordered = jnp.moveaxis(ordered, 0, concat_axis)
    shape = list(pieces[0].shape)
    shape[concat_axis] *= n_spec
    return ordered.reshape(shape)


def make_local(n_space, n_spec):
    both = ("space", "spec")
    n_all = n_space * n_spec

    def local(slm_phase, expander, phase_scale, target):
        waves = phase_scale.shape[0]
        rows_dev = expander.shape[0]
        rows_f = rows_dev // n_spec
        slm_rows = rows_f // 4
        lc = target.shape[1]
        cs = SUB // n_spec
        kk = lc * cs
        group = SUB // rows_f
        batch = waves * rows_f
        spec_index = lax.axis_index("spec")

        own_slm = spec_exchange(slm_phase, n_spec, 0, 1)
        own_exp = lax.dynamic_slice_in_dim(expander, spec_index * rows_f, rows_f, 0)

        slm_tile = own_slm.reshape(slm_rows, Q1, SUB // 4).transpose(0, 2, 1)
        upsampled = jnp.broadcast_to(
            slm_tile[:, None, :, None, :], (slm_rows, 4, SUB // 4, 4, Q1)
        ).reshape(rows_f, SUB, Q1)
        packed_words = own_exp.reshape(rows_f, Q1, SUB // 16).transpose(0, 2, 1)
        shifts = lax.broadcasted_iota(jnp.int32, (1, 1, 16, 1), 2)
        bit_values = jnp.bitwise_and(jnp.right_shift(packed_words[:, :, None, :], shifts), 1)
        expander_sign = (1 - 2 * bit_values).reshape(rows_f, SUB, Q1).astype(jnp.float32)
        phase_delay = phase_scale[:, None, None, None] * upsampled[None]
        near_real = (expander_sign[None] * jnp.cos(phase_delay)).astype(jnp.bfloat16)
        near_imag = (expander_sign[None] * jnp.sin(phase_delay)).astype(jnp.bfloat16)
        near_field = jnp.concatenate([near_real, near_imag], axis=-1).reshape(batch * SUB, 2 * Q1)

        outer_fwd = transform_block(Q1, False)
        outer_inv = transform_block(Q1, True)
        inner_fwd = transform_block(SUB, False)
        inner_inv = transform_block(SUB, True)
        row_cos, row_sin = angle_tables(SUB, Q1, N, 1.0)

        section_out = jnp.dot(near_field, outer_fwd, preferred_element_type=jnp.float32)
        section_out = section_out.reshape(batch, SUB, 2, Q1)
        first_real, first_imag = rotate_pair(
            section_out[:, :, 0], section_out[:, :, 1], row_cos, row_sin
        )
        first_part = jnp.stack([first_real, first_imag], axis=1).astype(jnp.bfloat16)
        first_part = first_part.reshape(batch, 2 * SUB, Q1)
        row_freq = jnp.einsum(
            "xk,bxa->kba", inner_fwd, first_part, preferred_element_type=jnp.float32
        ).astype(jnp.bfloat16)
        send = row_freq.reshape(2, n_spec, cs, batch, n_space, lc)
        send = send.transpose(4, 1, 0, 5, 2, 3).reshape(n_all, 16, -1)
        got = lax.all_to_all(send, both, split_axis=0, concat_axis=0, tiled=True)
        columns = got.reshape(Q1, group, 2, kk * batch).transpose(2, 0, 1, 3)
        columns = columns.reshape(2 * Q1, group * kk * batch)
        col_sec = jnp.einsum("xk,xy->ky", outer_fwd, columns, preferred_element_type=jnp.float32)
        col_sec = col_sec.reshape(2, Q1, group, kk * waves, rows_f)
        a2_index = lax.broadcasted_iota(jnp.int32, (Q1, group, 1, rows_f), 0)
        j2_index = (lax.broadcasted_iota(jnp.int32, (Q1, group, 1, rows_f), 1) * rows_f
                    + lax.broadcasted_iota(jnp.int32, (Q1, group, 1, rows_f), 3))
        col_angle = ((a2_index * j2_index) % N).astype(jnp.float32) * (2.0 * math.pi / N)
        g_cos = jnp.cos(col_angle) / N
        g_sin = -jnp.sin(col_angle) / N
        col_real, col_imag = rotate_pair(col_sec[0], col_sec[1], g_cos, g_sin)
        col_first = jnp.stack([col_real, col_imag], axis=0).astype(jnp.bfloat16)
        col_first = col_first.transpose(0, 2, 4, 3, 1).reshape(2 * SUB, kk * waves * Q1)
        far_field = jnp.dot(inner_inv, col_first, preferred_element_type=jnp.float32).astype(
            jnp.bfloat16
        )
        far_wide = far_field.astype(jnp.float32).reshape(2, SUB, kk, waves, Q1)
        power = jnp.sum(far_wide[0] * far_wide[0] + far_wide[1] * far_wide[1], axis=2)
        own_target = target.reshape(SUB, lc, n_spec, cs, Q1)
        own_target = lax.dynamic_index_in_dim(own_target, spec_index, 2, keepdims=False)
        residual = (power - own_target.reshape(SUB, kk, Q1)) / 32.0
        cotangent = (2.0 * residual[None, :, :, None] * far_wide).astype(jnp.bfloat16)
        back_out = jnp.dot(
            inner_fwd, cotangent.reshape(2 * SUB, kk * waves * Q1), preferred_element_type=jnp.float32
        ).reshape(2, SUB, kk * waves, Q1)
        gb_cos = g_cos.reshape(Q1, SUB).T[:, None, :]
        gb_sin = g_sin.reshape(Q1, SUB).T[:, None, :]
        back_real, back_imag = rotate_pair(back_out[0], back_out[1], gb_cos, -gb_sin)
        back_one = jnp.stack([back_real, back_imag], axis=0).astype(jnp.bfloat16)
        back_one = back_one.reshape(2, group, rows_f, kk, waves, Q1).transpose(0, 5, 1, 3, 2, 4)
        back_one = back_one.reshape(2 * Q1, group * kk * batch)
        back_two = jnp.einsum(
            "xk,xy->ky", outer_inv, back_one, preferred_element_type=jnp.float32
        ).astype(jnp.bfloat16)
        back_two = back_two.reshape(2, Q1, group, kk * batch).transpose(1, 2, 0, 3)
        rows_back = lax.all_to_all(
            back_two.reshape(n_all, 16, -1), both, split_axis=0, concat_axis=0, tiled=True
        )
        rows_back = rows_back.reshape(n_space, n_spec, 2, lc, cs, rows_f * waves)
        rows_back = rows_back.transpose(2, 1, 4, 5, 0, 3).reshape(2 * SUB, batch * Q1)
        section_out = jnp.einsum(
            "xk,xy->ky", inner_inv, rows_back, preferred_element_type=jnp.float32
        ).reshape(2, SUB, batch, Q1)
        rb_cos = row_cos[:, None, :]
        rb_sin = row_sin[:, None, :]
        turned_real, turned_imag = rotate_pair(section_out[0], section_out[1], rb_cos, -rb_sin)
        back_three = jnp.stack([turned_real, turned_imag], axis=0).astype(jnp.bfloat16)
        back_three = back_three.reshape(2, SUB, rows_f, waves, Q1).transpose(3, 2, 1, 0, 4)
        back_three = back_three.reshape(batch * SUB, 2 * Q1)
        near_grad = jnp.dot(back_three, outer_inv, preferred_element_type=jnp.float32).reshape(
            waves, rows_f, SUB, 2, Q1
        )
        near_wide = near_field.astype(jnp.float32).reshape(waves, rows_f, SUB, 2, Q1)
        slope = jnp.sum(
            phase_scale[:, None, None, None]
            * (near_grad[:, :, :, 1] * near_wide[:, :, :, 0] - near_grad[:, :, :, 0] * near_wide[:, :, :, 1]),
            axis=0,
        )
        pooled = slope.reshape(slm_rows, 4, SUB // 4, 4, Q1).sum(axis=(1, 3)).transpose(0, 2, 1)
        pooled = pooled.reshape(slm_rows, N // 4)
        return spec_exchange(pooled, n_spec, 1, 0)

    return local


def solution(mesh):
    return jax.shard_map(
        make_local(mesh.shape["space"], mesh.shape["spec"]),
        mesh=mesh,
        in_specs=(P("space", "spec"), P("space", None), P(), P(None, "space", None, None)),
        out_specs=P("space", "spec"),
        check_vma=False,
    )
```

```python
import math

import jax
import jax.numpy as jnp
from jax import lax
from jax.sharding import PartitionSpec as P

N = 8192
SUB = 64
Q1 = N // SUB


def angle_tables(first, second, length, scale):
    row_index = lax.broadcasted_iota(jnp.int32, (first, second), 0)
    col_index = lax.broadcasted_iota(jnp.int32, (first, second), 1)
    residue = (row_index * col_index % length).astype(jnp.float32)
    radians = residue * (2.0 * math.pi / length)
    return (jnp.cos(radians) * scale, -jnp.sin(radians) * scale)


def transform_block(length, conjugate):
    cos_part, sin_part = angle_tables(length, length, length, 1.0)
    cos_low = cos_part.astype(jnp.bfloat16)
    sin_low = sin_part.astype(jnp.bfloat16)
    if conjugate:
        sin_low = -sin_low
    upper = jnp.concatenate([cos_low, sin_low], axis=1)
    lower = jnp.concatenate([-sin_low, cos_low], axis=1)
    return jnp.concatenate([upper, lower], axis=0)


def rotate_pair(real_in, imag_in, cos_table, sin_table):
    return (real_in * cos_table - imag_in * sin_table, real_in * sin_table + imag_in * cos_table)


def make_local(n_space, n_spec):
    both = ("space", "spec")
    n_all = n_space * n_spec

    def local(slm_phase, expander, phase_scale, target):
        waves = phase_scale.shape[0]
        rows_dev = expander.shape[0]
        rows_f = rows_dev // n_spec
        slm_rows = rows_f // 4
        lc = target.shape[1]
        cs = SUB // n_spec
        kk = lc * cs
        group = SUB // rows_f
        batch = waves * rows_f
        spec_index = lax.axis_index("spec")

        own_slm = lax.all_to_all(slm_phase, "spec", split_axis=0, concat_axis=1, tiled=True)
        own_exp = lax.dynamic_slice_in_dim(expander, spec_index * rows_f, rows_f, 0)

        slm_tile = own_slm.reshape(slm_rows, Q1, SUB // 4).transpose(0, 2, 1)
        upsampled = jnp.broadcast_to(
            slm_tile[:, None, :, None, :], (slm_rows, 4, SUB // 4, 4, Q1)
        ).reshape(rows_f, SUB, Q1)
        packed_words = own_exp.reshape(rows_f, Q1, SUB // 16).transpose(0, 2, 1)
        shifts = lax.broadcasted_iota(jnp.int32, (1, 1, 16, 1), 2)
        bit_values = jnp.bitwise_and(jnp.right_shift(packed_words[:, :, None, :], shifts), 1)
        expander_sign = (1 - 2 * bit_values).reshape(rows_f, SUB, Q1).astype(jnp.float32)
        phase_delay = phase_scale[:, None, None, None] * upsampled[None]
        near_real = (expander_sign[None] * jnp.cos(phase_delay)).astype(jnp.bfloat16)
        near_imag = (expander_sign[None] * jnp.sin(phase_delay)).astype(jnp.bfloat16)
        near_field = jnp.concatenate([near_real, near_imag], axis=-1).reshape(batch * SUB, 2 * Q1)

        outer_fwd = transform_block(Q1, False)
        outer_inv = transform_block(Q1, True)
        inner_fwd = transform_block(SUB, False)
        inner_inv = transform_block(SUB, True)
        row_cos, row_sin = angle_tables(SUB, Q1, N, 1.0)

        section_out = jnp.dot(near_field, outer_fwd, preferred_element_type=jnp.bfloat16)
        section_out = section_out.reshape(batch, SUB, 2, Q1)
        first_real, first_imag = rotate_pair(
            section_out[:, :, 0], section_out[:, :, 1], row_cos, row_sin
        )
        first_part = jnp.stack([first_real, first_imag], axis=1).astype(jnp.bfloat16)
        first_part = first_part.reshape(batch, 2 * SUB, Q1)
        row_freq = jnp.einsum(
            "xk,bxa->kba", inner_fwd, first_part, preferred_element_type=jnp.float32
        ).astype(jnp.bfloat16)
        send = row_freq.reshape(2, n_spec, cs, batch, n_space, lc)
        send = send.transpose(4, 1, 0, 5, 2, 3).reshape(n_all, 16, -1)
        got = lax.all_to_all(send, both, split_axis=0, concat_axis=0, tiled=True)
        columns = got.reshape(Q1, group, 2, kk * batch).transpose(2, 0, 1, 3)
        columns = columns.reshape(2 * Q1, group * kk * batch)
        col_sec = jnp.einsum("xk,xy->ky", outer_fwd, columns, preferred_element_type=jnp.bfloat16)
        col_sec = col_sec.reshape(2, Q1, group, kk * waves, rows_f)
        a2_index = lax.broadcasted_iota(jnp.int32, (Q1, group, 1, rows_f), 0)
        j2_index = (lax.broadcasted_iota(jnp.int32, (Q1, group, 1, rows_f), 1) * rows_f
                    + lax.broadcasted_iota(jnp.int32, (Q1, group, 1, rows_f), 3))
        col_angle = ((a2_index * j2_index) % N).astype(jnp.float32) * (2.0 * math.pi / N)
        g_cos = jnp.cos(col_angle) / N
        g_sin = -jnp.sin(col_angle) / N
        col_real, col_imag = rotate_pair(col_sec[0], col_sec[1], g_cos, g_sin)
        col_first = jnp.stack([col_real, col_imag], axis=0).astype(jnp.bfloat16)
        col_first = col_first.transpose(0, 2, 4, 3, 1).reshape(2 * SUB, kk * waves * Q1)
        far_field = jnp.dot(inner_inv, col_first, preferred_element_type=jnp.float32).astype(
            jnp.bfloat16
        )
        far_wide = far_field.astype(jnp.float32).reshape(2, SUB, kk, waves, Q1)
        power = jnp.sum(far_wide[0] * far_wide[0] + far_wide[1] * far_wide[1], axis=2)
        own_target = target.reshape(SUB, lc, n_spec, cs, Q1)
        own_target = lax.dynamic_index_in_dim(own_target, spec_index, 2, keepdims=False)
        residual = (power - own_target.reshape(SUB, kk, Q1)) / 32.0
        cotangent = (2.0 * residual[None, :, :, None] * far_wide).astype(jnp.bfloat16)
        back_out = jnp.dot(
            inner_fwd, cotangent.reshape(2 * SUB, kk * waves * Q1), preferred_element_type=jnp.bfloat16
        ).reshape(2, SUB, kk * waves, Q1)
        gb_cos = g_cos.reshape(Q1, SUB).T[:, None, :]
        gb_sin = g_sin.reshape(Q1, SUB).T[:, None, :]
        back_real, back_imag = rotate_pair(back_out[0], back_out[1], gb_cos, -gb_sin)
        back_one = jnp.stack([back_real, back_imag], axis=0).astype(jnp.bfloat16)
        back_one = back_one.reshape(2, group, rows_f, kk, waves, Q1).transpose(0, 5, 1, 3, 2, 4)
        back_one = back_one.reshape(2 * Q1, group * kk * batch)
        back_two = jnp.einsum(
            "xk,xy->ky", outer_inv, back_one, preferred_element_type=jnp.float32
        ).astype(jnp.bfloat16)
        back_two = back_two.reshape(2, Q1, group, kk * batch).transpose(1, 2, 0, 3)
        rows_back = lax.all_to_all(
            back_two.reshape(n_all, 16, -1), both, split_axis=0, concat_axis=0, tiled=True
        )
        rows_back = rows_back.reshape(n_space, n_spec, 2, lc, cs, rows_f * waves)
        rows_back = rows_back.transpose(2, 1, 4, 5, 0, 3).reshape(2 * SUB, batch * Q1)
        section_out = jnp.einsum(
            "xk,xy->ky", inner_inv, rows_back, preferred_element_type=jnp.bfloat16
        ).reshape(2, SUB, batch, Q1)
        rb_cos = row_cos[:, None, :]
        rb_sin = row_sin[:, None, :]
        turned_real, turned_imag = rotate_pair(section_out[0], section_out[1], rb_cos, -rb_sin)
        back_three = jnp.stack([turned_real, turned_imag], axis=0).astype(jnp.bfloat16)
        back_three = back_three.reshape(2, SUB, rows_f, waves, Q1).transpose(3, 2, 1, 0, 4)
        back_three = back_three.reshape(batch * SUB, 2 * Q1)
        near_grad = jnp.dot(back_three, outer_inv, preferred_element_type=jnp.float32).reshape(
            waves, rows_f, SUB, 2, Q1
        )
        near_wide = near_field.astype(jnp.float32).reshape(waves, rows_f, SUB, 2, Q1)
        slope = jnp.sum(
            phase_scale[:, None, None, None]
            * (near_grad[:, :, :, 1] * near_wide[:, :, :, 0] - near_grad[:, :, :, 0] * near_wide[:, :, :, 1]),
            axis=0,
        )
        pooled = slope.reshape(slm_rows, 4, SUB // 4, 4, Q1).sum(axis=(1, 3)).transpose(0, 2, 1)
        pooled = pooled.reshape(slm_rows, N // 4)
        return lax.all_to_all(pooled, "spec", split_axis=1, concat_axis=0, tiled=True)

    return local


def solution(mesh):
    return jax.shard_map(
        make_local(mesh.shape["space"], mesh.shape["spec"]),
        mesh=mesh,
        in_specs=(P("space", "spec"), P("space", None), P(), P(None, "space", None, None)),
        out_specs=P("space", "spec"),
        check_vma=False,
    )
```

```python
import math

import jax
import jax.numpy as jnp
from jax import lax
from jax.sharding import PartitionSpec as P

N = 8192
SUB = 64
Q1 = N // SUB


def angle_tables(first, second, length, scale):
    row_index = lax.broadcasted_iota(jnp.int32, (first, second), 0)
    col_index = lax.broadcasted_iota(jnp.int32, (first, second), 1)
    residue = (row_index * col_index % length).astype(jnp.float32)
    radians = residue * (2.0 * math.pi / length)
    return (jnp.cos(radians) * scale, -jnp.sin(radians) * scale)


def transform_block(length, conjugate):
    cos_part, sin_part = angle_tables(length, length, length, 1.0)
    cos_low = cos_part.astype(jnp.bfloat16)
    sin_low = sin_part.astype(jnp.bfloat16)
    if conjugate:
        sin_low = -sin_low
    upper = jnp.concatenate([cos_low, sin_low], axis=1)
    lower = jnp.concatenate([-sin_low, cos_low], axis=1)
    return jnp.concatenate([upper, lower], axis=0)


def rotate_pair(real_in, imag_in, cos_table, sin_table):
    return (real_in * cos_table - imag_in * sin_table, real_in * sin_table + imag_in * cos_table)


def make_local(n_space, n_spec):
    both = ("space", "spec")
    n_all = n_space * n_spec

    def local(slm_phase, expander, phase_scale, target):
        waves = phase_scale.shape[0]
        rows_dev = expander.shape[0]
        rows_f = rows_dev // n_spec
        slm_rows = rows_f // 4
        lc = target.shape[1]
        cs = SUB // n_spec
        kk = lc * cs
        group = SUB // rows_f
        batch = waves * rows_f
        spec_index = lax.axis_index("spec")

        own_slm = lax.all_to_all(slm_phase, "spec", split_axis=0, concat_axis=1, tiled=True)
        own_exp = lax.dynamic_slice_in_dim(expander, spec_index * rows_f, rows_f, 0)

        slm_delay = phase_scale[:, None, None] * own_slm[None]

        def upsample(per_pixel):
            tile = per_pixel.reshape(waves, slm_rows, Q1, SUB // 4).transpose(0, 1, 3, 2)
            return jnp.broadcast_to(
                tile[:, :, None, :, None, :], (waves, slm_rows, 4, SUB // 4, 4, Q1)
            ).reshape(waves, rows_f, SUB, Q1)

        packed_words = own_exp.reshape(rows_f, Q1, SUB // 16).transpose(0, 2, 1)
        shifts = lax.broadcasted_iota(jnp.int32, (1, 1, 16, 1), 2)
        bit_values = jnp.bitwise_and(jnp.right_shift(packed_words[:, :, None, :], shifts), 1)
        expander_sign = (1 - 2 * bit_values).reshape(rows_f, SUB, Q1).astype(jnp.float32)
        near_real = (expander_sign[None] * upsample(jnp.cos(slm_delay))).astype(jnp.bfloat16)
        near_imag = (expander_sign[None] * upsample(jnp.sin(slm_delay))).astype(jnp.bfloat16)
        near_field = jnp.concatenate([near_real, near_imag], axis=-1).reshape(batch * SUB, 2 * Q1)

        outer_fwd = transform_block(Q1, False)
        outer_inv = transform_block(Q1, True)
        inner_fwd = transform_block(SUB, False)
        inner_inv = transform_block(SUB, True)
        row_cos, row_sin = angle_tables(SUB, Q1, N, 1.0)

        section_out = jnp.dot(near_field, outer_fwd, preferred_element_type=jnp.float32)
        section_out = section_out.reshape(batch, SUB, 2, Q1)
        first_real, first_imag = rotate_pair(
            section_out[:, :, 0], section_out[:, :, 1], row_cos, row_sin
        )
        first_part = jnp.stack([first_real, first_imag], axis=1).astype(jnp.bfloat16)
        first_part = first_part.reshape(batch, 2 * SUB, Q1)
        row_freq = jnp.einsum(
            "xk,bxa->kba", inner_fwd, first_part, preferred_element_type=jnp.float32
        ).astype(jnp.bfloat16)
        send = row_freq.reshape(2, n_spec, cs, batch, n_space, lc)
        send = send.transpose(4, 1, 0, 5, 2, 3).reshape(n_all, 16, -1)
        got = lax.all_to_all(send, both, split_axis=0, concat_axis=0, tiled=True)
        columns = got.reshape(Q1, group, 2, kk * batch).transpose(2, 0, 1, 3)
        columns = columns.reshape(2 * Q1, group * kk * batch)
        col_sec = jnp.einsum("xk,xy->ky", outer_fwd, columns, preferred_element_type=jnp.float32)
        col_sec = col_sec.reshape(2, Q1, group, kk * waves, rows_f)
        a2_index = lax.broadcasted_iota(jnp.int32, (Q1, group, 1, rows_f), 0)
        j2_index = (lax.broadcasted_iota(jnp.int32, (Q1, group, 1, rows_f), 1) * rows_f
                    + lax.broadcasted_iota(jnp.int32, (Q1, group, 1, rows_f), 3))
        col_angle = ((a2_index * j2_index) % N).astype(jnp.float32) * (2.0 * math.pi / N)
        g_cos = jnp.cos(col_angle) / N
        g_sin = -jnp.sin(col_angle) / N
        col_real, col_imag = rotate_pair(col_sec[0], col_sec[1], g_cos, g_sin)
        col_first = jnp.stack([col_real, col_imag], axis=0).astype(jnp.bfloat16)
        col_first = col_first.transpose(0, 2, 4, 3, 1).reshape(2 * SUB, kk * waves * Q1)
        far_field = jnp.dot(inner_inv, col_first, preferred_element_type=jnp.float32).astype(
            jnp.bfloat16
        )
        far_wide = far_field.astype(jnp.float32).reshape(2, SUB, kk, waves, Q1)
        power = jnp.sum(far_wide[0] * far_wide[0] + far_wide[1] * far_wide[1], axis=2)
        own_target = target.reshape(SUB, lc, n_spec, cs, Q1)
        own_target = lax.dynamic_index_in_dim(own_target, spec_index, 2, keepdims=False)
        residual = (power - own_target.reshape(SUB, kk, Q1)) / 32.0
        cotangent = (2.0 * residual[None, :, :, None] * far_wide).astype(jnp.bfloat16)
        back_out = jnp.dot(
            inner_fwd, cotangent.reshape(2 * SUB, kk * waves * Q1), preferred_element_type=jnp.float32
        ).reshape(2, SUB, kk * waves, Q1)
        gb_cos = g_cos.reshape(Q1, SUB).T[:, None, :]
        gb_sin = g_sin.reshape(Q1, SUB).T[:, None, :]
        back_real, back_imag = rotate_pair(back_out[0], back_out[1], gb_cos, -gb_sin)
        back_one = jnp.stack([back_real, back_imag], axis=0).astype(jnp.bfloat16)
        back_one = back_one.reshape(2, group, rows_f, kk, waves, Q1).transpose(0, 5, 1, 3, 2, 4)
        back_one = back_one.reshape(2 * Q1, group * kk * batch)
        back_two = jnp.einsum(
            "xk,xy->ky", outer_inv, back_one, preferred_element_type=jnp.float32
        ).astype(jnp.bfloat16)
        back_two = back_two.reshape(2, Q1, group, kk * batch).transpose(1, 2, 0, 3)
        rows_back = lax.all_to_all(
            back_two.reshape(n_all, 16, -1), both, split_axis=0, concat_axis=0, tiled=True
        )
        rows_back = rows_back.reshape(n_space, n_spec, 2, lc, cs, rows_f * waves)
        rows_back = rows_back.transpose(2, 1, 4, 5, 0, 3).reshape(2 * SUB, batch * Q1)
        section_out = jnp.einsum(
            "xk,xy->ky", inner_inv, rows_back, preferred_element_type=jnp.float32
        ).reshape(2, SUB, batch, Q1)
        rb_cos = row_cos[:, None, :]
        rb_sin = row_sin[:, None, :]
        turned_real, turned_imag = rotate_pair(section_out[0], section_out[1], rb_cos, -rb_sin)
        back_three = jnp.stack([turned_real, turned_imag], axis=0).astype(jnp.bfloat16)
        back_three = back_three.reshape(2, SUB, rows_f, waves, Q1).transpose(3, 2, 1, 0, 4)
        back_three = back_three.reshape(batch * SUB, 2 * Q1)
        near_grad = jnp.dot(back_three, outer_inv, preferred_element_type=jnp.float32).reshape(
            waves, rows_f, SUB, 2, Q1
        )
        near_wide = near_field.astype(jnp.float32).reshape(waves, rows_f, SUB, 2, Q1)
        slope = jnp.sum(
            phase_scale[:, None, None, None]
            * (near_grad[:, :, :, 1] * near_wide[:, :, :, 0] - near_grad[:, :, :, 0] * near_wide[:, :, :, 1]),
            axis=0,
        )
        pooled = slope.reshape(slm_rows, 4, SUB // 4, 4, Q1).sum(axis=(1, 3)).transpose(0, 2, 1)
        pooled = pooled.reshape(slm_rows, N // 4)
        return lax.all_to_all(pooled, "spec", split_axis=1, concat_axis=0, tiled=True)

    return local


def solution(mesh):
    return jax.shard_map(
        make_local(mesh.shape["space"], mesh.shape["spec"]),
        mesh=mesh,
        in_specs=(P("space", "spec"), P("space", None), P(), P(None, "space", None, None)),
        out_specs=P("space", "spec"),
        check_vma=False,
    )
```

```python
import math

import jax
import jax.numpy as jnp
from jax import lax
from jax.sharding import PartitionSpec as P

N = 8192
SUB = 64
Q1 = N // SUB


def angle_tables(first, second, length, scale):
    row_index = lax.broadcasted_iota(jnp.int32, (first, second), 0)
    col_index = lax.broadcasted_iota(jnp.int32, (first, second), 1)
    residue = (row_index * col_index % length).astype(jnp.float32)
    radians = residue * (2.0 * math.pi / length)
    return (jnp.cos(radians) * scale, -jnp.sin(radians) * scale)


def transform_block(length, conjugate):
    cos_part, sin_part = angle_tables(length, length, length, 1.0)
    cos_low = cos_part.astype(jnp.bfloat16)
    sin_low = sin_part.astype(jnp.bfloat16)
    if conjugate:
        sin_low = -sin_low
    upper = jnp.concatenate([cos_low, sin_low], axis=1)
    lower = jnp.concatenate([-sin_low, cos_low], axis=1)
    return jnp.concatenate([upper, lower], axis=0)


def rotate_pair(real_in, imag_in, cos_table, sin_table):
    return (real_in * cos_table - imag_in * sin_table, real_in * sin_table + imag_in * cos_table)


def make_local(n_space, n_spec):
    both = ("space", "spec")
    n_all = n_space * n_spec

    def local(slm_phase, expander, phase_scale, target):
        waves = phase_scale.shape[0]
        rows_dev = expander.shape[0]
        rows_f = rows_dev // n_spec
        slm_rows = rows_f // 4
        lc = target.shape[1]
        cs = SUB // n_spec
        kk = lc * cs
        group = SUB // rows_f
        batch = waves * rows_f
        spec_index = lax.axis_index("spec")

        own_slm = lax.all_to_all(slm_phase, "spec", split_axis=0, concat_axis=1, tiled=True)
        own_exp = lax.dynamic_slice_in_dim(expander, spec_index * rows_f, rows_f, 0)


        def upsample(per_pixel):
            tile = per_pixel.reshape(waves, slm_rows, Q1, SUB // 4).transpose(0, 1, 3, 2)
            return jnp.broadcast_to(
                tile[:, :, None, :, None, :], (waves, slm_rows, 4, SUB // 4, 4, Q1)
            ).reshape(waves, rows_f, SUB, Q1)

        def make_near(slm_in, exp_in):
            slm_delay = phase_scale[:, None, None] * slm_in[None]
            packed_words = exp_in.reshape(rows_f, Q1, SUB // 16).transpose(0, 2, 1)
            shifts = lax.broadcasted_iota(jnp.int32, (1, 1, 16, 1), 2)
            bit_values = jnp.bitwise_and(jnp.right_shift(packed_words[:, :, None, :], shifts), 1)
            expander_sign = (1 - 2 * bit_values).reshape(rows_f, SUB, Q1).astype(jnp.float32)
            near_real = (expander_sign[None] * upsample(jnp.cos(slm_delay))).astype(jnp.bfloat16)
            near_imag = (expander_sign[None] * upsample(jnp.sin(slm_delay))).astype(jnp.bfloat16)
            near = jnp.concatenate([near_real, near_imag], axis=-1)
            return near.reshape(batch * SUB, 2 * Q1)

        near_field = make_near(own_slm, own_exp)

        outer_fwd = transform_block(Q1, False)
        outer_inv = transform_block(Q1, True)
        inner_fwd = transform_block(SUB, False)
        inner_inv = transform_block(SUB, True)
        row_cos, row_sin = angle_tables(SUB, Q1, N, 1.0)

        section_out = jnp.dot(near_field, outer_fwd, preferred_element_type=jnp.float32)
        section_out = section_out.reshape(batch, SUB, 2, Q1)
        first_real, first_imag = rotate_pair(
            section_out[:, :, 0], section_out[:, :, 1], row_cos, row_sin
        )
        first_part = jnp.stack([first_real, first_imag], axis=1).astype(jnp.bfloat16)
        first_part = first_part.reshape(batch, 2 * SUB, Q1)
        row_freq = jnp.einsum(
            "xk,bxa->kba", inner_fwd, first_part, preferred_element_type=jnp.float32
        ).astype(jnp.bfloat16)
        send = row_freq.reshape(2, n_spec, cs, batch, n_space, lc)
        send = send.transpose(4, 1, 0, 5, 2, 3).reshape(n_all, 16, -1)
        got = lax.all_to_all(send, both, split_axis=0, concat_axis=0, tiled=True)
        columns = got.reshape(Q1, group, 2, kk * batch).transpose(2, 0, 1, 3)
        columns = columns.reshape(2 * Q1, group * kk * batch)
        col_sec = jnp.einsum("xk,xy->ky", outer_fwd, columns, preferred_element_type=jnp.float32)
        col_sec = col_sec.reshape(2, Q1, group, kk * waves, rows_f)
        a2_index = lax.broadcasted_iota(jnp.int32, (Q1, group, 1, rows_f), 0)
        j2_index = (lax.broadcasted_iota(jnp.int32, (Q1, group, 1, rows_f), 1) * rows_f
                    + lax.broadcasted_iota(jnp.int32, (Q1, group, 1, rows_f), 3))
        col_angle = ((a2_index * j2_index) % N).astype(jnp.float32) * (2.0 * math.pi / N)
        g_cos = jnp.cos(col_angle) / N
        g_sin = -jnp.sin(col_angle) / N
        col_real, col_imag = rotate_pair(col_sec[0], col_sec[1], g_cos, g_sin)
        col_first = jnp.stack([col_real, col_imag], axis=0).astype(jnp.bfloat16)
        col_first = col_first.transpose(0, 2, 4, 3, 1).reshape(2 * SUB, kk * waves * Q1)
        far_field = jnp.dot(inner_inv, col_first, preferred_element_type=jnp.float32).astype(
            jnp.bfloat16
        )
        far_wide = far_field.astype(jnp.float32).reshape(2, SUB, kk, waves, Q1)
        power = jnp.sum(far_wide[0] * far_wide[0] + far_wide[1] * far_wide[1], axis=2)
        own_target = target.reshape(SUB, lc, n_spec, cs, Q1)
        own_target = lax.dynamic_index_in_dim(own_target, spec_index, 2, keepdims=False)
        residual = (power - own_target.reshape(SUB, kk, Q1)) / 32.0
        cotangent = (2.0 * residual[None, :, :, None] * far_wide).astype(jnp.bfloat16)
        back_out = jnp.dot(
            inner_fwd, cotangent.reshape(2 * SUB, kk * waves * Q1), preferred_element_type=jnp.float32
        ).reshape(2, SUB, kk * waves, Q1)
        gb_cos = g_cos.reshape(Q1, SUB).T[:, None, :]
        gb_sin = g_sin.reshape(Q1, SUB).T[:, None, :]
        back_real, back_imag = rotate_pair(back_out[0], back_out[1], gb_cos, -gb_sin)
        back_one = jnp.stack([back_real, back_imag], axis=0).astype(jnp.bfloat16)
        back_one = back_one.reshape(2, group, rows_f, kk, waves, Q1).transpose(0, 5, 1, 3, 2, 4)
        back_one = back_one.reshape(2 * Q1, group * kk * batch)
        back_two = jnp.einsum(
            "xk,xy->ky", outer_inv, back_one, preferred_element_type=jnp.float32
        ).astype(jnp.bfloat16)
        back_two = back_two.reshape(2, Q1, group, kk * batch).transpose(1, 2, 0, 3)
        send_back, slm_again, exp_again = lax.optimization_barrier(
            (back_two.reshape(n_all, 16, -1), own_slm, own_exp)
        )
        rows_back = lax.all_to_all(send_back, both, split_axis=0, concat_axis=0, tiled=True)
        near_again = lax.optimization_barrier(make_near(slm_again, exp_again))
        rows_back = rows_back.reshape(n_space, n_spec, 2, lc, cs, rows_f * waves)
        rows_back = rows_back.transpose(2, 1, 4, 5, 0, 3).reshape(2 * SUB, batch * Q1)
        section_out = jnp.einsum(
            "xk,xy->ky", inner_inv, rows_back, preferred_element_type=jnp.float32
        ).reshape(2, SUB, batch, Q1)
        rb_cos = row_cos[:, None, :]
        rb_sin = row_sin[:, None, :]
        turned_real, turned_imag = rotate_pair(section_out[0], section_out[1], rb_cos, -rb_sin)
        back_three = jnp.stack([turned_real, turned_imag], axis=0).astype(jnp.bfloat16)
        back_three = back_three.reshape(2, SUB, rows_f, waves, Q1).transpose(3, 2, 1, 0, 4)
        back_three = back_three.reshape(batch * SUB, 2 * Q1)
        near_grad = jnp.dot(back_three, outer_inv, preferred_element_type=jnp.float32).reshape(
            waves, rows_f, SUB, 2, Q1
        )
        near_wide = near_again.astype(jnp.float32).reshape(waves, rows_f, SUB, 2, Q1)
        slope = jnp.sum(
            phase_scale[:, None, None, None]
            * (near_grad[:, :, :, 1] * near_wide[:, :, :, 0] - near_grad[:, :, :, 0] * near_wide[:, :, :, 1]),
            axis=0,
        )
        pooled = slope.reshape(slm_rows, 4, SUB // 4, 4, Q1).sum(axis=(1, 3)).transpose(0, 2, 1)
        pooled = pooled.reshape(slm_rows, N // 4)
        return lax.all_to_all(pooled, "spec", split_axis=1, concat_axis=0, tiled=True)

    return local


def solution(mesh):
    return jax.shard_map(
        make_local(mesh.shape["space"], mesh.shape["spec"]),
        mesh=mesh,
        in_specs=(P("space", "spec"), P("space", None), P(), P(None, "space", None, None)),
        out_specs=P("space", "spec"),
        check_vma=False,
    )
```

```python
import math

import jax
import jax.numpy as jnp
from jax import lax
from jax.sharding import PartitionSpec as P

N = 8192
SUB = 64
Q1 = N // SUB


def angle_tables(first, second, length, scale):
    row_index = lax.broadcasted_iota(jnp.int32, (first, second), 0)
    col_index = lax.broadcasted_iota(jnp.int32, (first, second), 1)
    residue = (row_index * col_index % length).astype(jnp.float32)
    radians = residue * (2.0 * math.pi / length)
    return (jnp.cos(radians) * scale, -jnp.sin(radians) * scale)


def transform_block(length, conjugate):
    cos_part, sin_part = angle_tables(length, length, length, 1.0)
    cos_low = cos_part.astype(jnp.bfloat16)
    sin_low = sin_part.astype(jnp.bfloat16)
    if conjugate:
        sin_low = -sin_low
    upper = jnp.concatenate([cos_low, sin_low], axis=1)
    lower = jnp.concatenate([-sin_low, cos_low], axis=1)
    return jnp.concatenate([upper, lower], axis=0)


def rotate_pair(real_in, imag_in, cos_table, sin_table):
    return (real_in * cos_table - imag_in * sin_table, real_in * sin_table + imag_in * cos_table)


def make_local(n_space, n_spec):
    both = ("space", "spec")
    n_all = n_space * n_spec

    def local(slm_phase, expander, phase_scale, target):
        waves = phase_scale.shape[0]
        rows_dev = expander.shape[0]
        rows_f = rows_dev // n_spec
        slm_rows = rows_f // 4
        lc = target.shape[1]
        cs = SUB // n_spec
        kk = lc * cs
        group = SUB // rows_f
        batch = waves * rows_f
        spec_index = lax.axis_index("spec")

        own_slm = lax.all_to_all(slm_phase, "spec", split_axis=0, concat_axis=1, tiled=True)
        own_exp = lax.dynamic_slice_in_dim(expander, spec_index * rows_f, rows_f, 0)


        def upsample(per_pixel):
            tile = per_pixel.reshape(waves, slm_rows, Q1, SUB // 4).transpose(0, 1, 3, 2)
            return jnp.broadcast_to(
                tile[:, :, None, :, None, :], (waves, slm_rows, 4, SUB // 4, 4, Q1)
            ).reshape(waves, rows_f, SUB, Q1)

        def make_near(slm_in, exp_in):
            slm_delay = phase_scale[:, None, None] * slm_in[None]
            packed_words = exp_in.reshape(rows_f, Q1, SUB // 16).transpose(0, 2, 1)
            shifts = lax.broadcasted_iota(jnp.int32, (1, 1, 16, 1), 2)
            bit_values = jnp.bitwise_and(jnp.right_shift(packed_words[:, :, None, :], shifts), 1)
            expander_sign = (1 - 2 * bit_values).reshape(rows_f, SUB, Q1).astype(jnp.float32)
            near_real = (expander_sign[None] * upsample(jnp.cos(slm_delay))).astype(jnp.bfloat16)
            near_imag = (expander_sign[None] * upsample(jnp.sin(slm_delay))).astype(jnp.bfloat16)
            near = jnp.concatenate([near_real, near_imag], axis=-1)
            return near.reshape(batch * SUB, 2 * Q1)

        near_field = make_near(own_slm, own_exp)

        outer_fwd = transform_block(Q1, False)
        outer_inv = transform_block(Q1, True)
        inner_fwd = transform_block(SUB, False)
        inner_inv = transform_block(SUB, True)
        row_cos, row_sin = angle_tables(SUB, Q1, N, 1.0)

        section_out = jnp.dot(near_field, outer_fwd, preferred_element_type=jnp.float32)
        section_out = section_out.reshape(batch, SUB, 2, Q1)
        first_real, first_imag = rotate_pair(
            section_out[:, :, 0], section_out[:, :, 1], row_cos, row_sin
        )
        first_part = jnp.stack([first_real, first_imag], axis=1).astype(jnp.bfloat16)
        first_part = first_part.reshape(batch, 2 * SUB, Q1)
        row_freq = jnp.einsum(
            "xk,bxa->kba", inner_fwd, first_part, preferred_element_type=jnp.float32
        ).astype(jnp.bfloat16)
        send = row_freq.reshape(2, n_spec, cs, batch, n_space, lc)
        send = send.transpose(4, 1, 0, 5, 2, 3).reshape(n_all, 16, -1)
        got = lax.all_to_all(send, both, split_axis=0, concat_axis=0, tiled=True)
        columns = got.reshape(Q1, group, 2, kk * batch).transpose(2, 0, 1, 3)
        columns = columns.reshape(2 * Q1, group * kk * batch)
        col_sec = jnp.einsum("xk,xy->ky", outer_fwd, columns, preferred_element_type=jnp.float32)
        col_sec = col_sec.reshape(2, Q1, group, kk * waves, rows_f)
        a2_index = lax.broadcasted_iota(jnp.int32, (Q1, group, 1, rows_f), 0)
        j2_index = (lax.broadcasted_iota(jnp.int32, (Q1, group, 1, rows_f), 1) * rows_f
                    + lax.broadcasted_iota(jnp.int32, (Q1, group, 1, rows_f), 3))
        col_angle = ((a2_index * j2_index) % N).astype(jnp.float32) * (2.0 * math.pi / N)
        g_cos = jnp.cos(col_angle) / N
        g_sin = -jnp.sin(col_angle) / N
        col_real, col_imag = rotate_pair(col_sec[0], col_sec[1], g_cos, g_sin)
        col_first = jnp.stack([col_real, col_imag], axis=0).astype(jnp.bfloat16)
        col_first = col_first.transpose(0, 2, 4, 3, 1).reshape(2 * SUB, kk * waves * Q1)
        far_field = jnp.dot(inner_inv, col_first, preferred_element_type=jnp.float32).astype(
            jnp.bfloat16
        )
        far_wide = far_field.astype(jnp.float32).reshape(2, SUB, kk, waves, Q1)
        power = jnp.sum(far_wide[0] * far_wide[0] + far_wide[1] * far_wide[1], axis=2)
        own_target = target.reshape(SUB, lc, n_spec, cs, Q1)
        own_target = lax.dynamic_index_in_dim(own_target, spec_index, 2, keepdims=False)
        residual = (power - own_target.reshape(SUB, kk, Q1)) / 32.0
        cotangent = (2.0 * residual[None, :, :, None] * far_wide).astype(jnp.bfloat16)
        cotangent = lax.optimization_barrier(cotangent)
        back_out = jnp.dot(
            inner_fwd, cotangent.reshape(2 * SUB, kk * waves * Q1), preferred_element_type=jnp.float32
        ).reshape(2, SUB, kk * waves, Q1)
        gb_cos = g_cos.reshape(Q1, SUB).T[:, None, :]
        gb_sin = g_sin.reshape(Q1, SUB).T[:, None, :]
        back_real, back_imag = rotate_pair(back_out[0], back_out[1], gb_cos, -gb_sin)
        back_one = jnp.stack([back_real, back_imag], axis=0).astype(jnp.bfloat16)
        back_one = back_one.reshape(2, group, rows_f, kk, waves, Q1).transpose(0, 5, 1, 3, 2, 4)
        back_one = back_one.reshape(2 * Q1, group * kk * batch)
        back_two = jnp.einsum(
            "xk,xy->ky", outer_inv, back_one, preferred_element_type=jnp.float32
        ).astype(jnp.bfloat16)
        back_two = back_two.reshape(2, Q1, group, kk * batch).transpose(1, 2, 0, 3)
        send_back, slm_again, exp_again = lax.optimization_barrier(
            (back_two.reshape(n_all, 16, -1), own_slm, own_exp)
        )
        rows_back = lax.all_to_all(send_back, both, split_axis=0, concat_axis=0, tiled=True)
        near_again = lax.optimization_barrier(make_near(slm_again, exp_again))
        rows_back = rows_back.reshape(n_space, n_spec, 2, lc, cs, rows_f * waves)
        rows_back = rows_back.transpose(2, 1, 4, 5, 0, 3).reshape(2 * SUB, batch * Q1)
        section_out = jnp.einsum(
            "xk,xy->ky", inner_inv, rows_back, preferred_element_type=jnp.float32
        ).reshape(2, SUB, batch, Q1)
        rb_cos = row_cos[:, None, :]
        rb_sin = row_sin[:, None, :]
        turned_real, turned_imag = rotate_pair(section_out[0], section_out[1], rb_cos, -rb_sin)
        back_three = jnp.stack([turned_real, turned_imag], axis=0).astype(jnp.bfloat16)
        back_three = back_three.reshape(2, SUB, rows_f, waves, Q1).transpose(3, 2, 1, 0, 4)
        back_three = back_three.reshape(batch * SUB, 2 * Q1)
        near_grad = jnp.dot(back_three, outer_inv, preferred_element_type=jnp.float32).reshape(
            waves, rows_f, SUB, 2, Q1
        )
        near_wide = near_again.astype(jnp.float32).reshape(waves, rows_f, SUB, 2, Q1)
        slope = jnp.sum(
            phase_scale[:, None, None, None]
            * (near_grad[:, :, :, 1] * near_wide[:, :, :, 0] - near_grad[:, :, :, 0] * near_wide[:, :, :, 1]),
            axis=0,
        )
        pooled = slope.reshape(slm_rows, 4, SUB // 4, 4, Q1).sum(axis=(1, 3)).transpose(0, 2, 1)
        pooled = pooled.reshape(slm_rows, N // 4)
        return lax.all_to_all(pooled, "spec", split_axis=1, concat_axis=0, tiled=True)

    return local


def solution(mesh):
    return jax.shard_map(
        make_local(mesh.shape["space"], mesh.shape["spec"]),
        mesh=mesh,
        in_specs=(P("space", "spec"), P("space", None), P(), P(None, "space", None, None)),
        out_specs=P("space", "spec"),
        check_vma=False,
    )
```
